32 devices in a mesh: group: 2 (over y), ctx: 4 (over z), head: 2 (over x), sub: 2 (over core).
Axes of the slice: x: 2, y: 2, z: 4, core: 2. Of those that a mesh axis runs over, the one named last changes fastest.
Arguments:
- queries: bfloat16 [4, 4096, 128], P(('head', 'sub'), ('group', 'ctx')), parts along dimension 1, may hold values from -18 to 18
- keys: bfloat16 [4, 4096, 128], P(('head', 'sub'), ('group', 'ctx')), parts along dimension 1, may hold values from -6 to 6
- values: bfloat16 [4, 4096, 128], P(('head', 'sub'), ('group', 'ctx')), parts along dimension 1, may hold values from -6 to 6
- stick_offset: float32 [4], P(('head', 'sub')), may hold values from -14 to -7
Outputs:
- attended: bfloat16 [4, 4096, 128], P(('head', 'sub'), ('group', 'ctx')), parts along dimension 1
The draws below stay inside these ranges and needn't reach their ends.
There are 2 independent parts, one for each index of `group`. The reference program is written for one: setup_inputs(seed, part) draws one part's arguments, and reference() takes and returns one part's arrays. A program takes and returns all parts, laid end to end along the dimension named above; an argument that names none is the same for every part. Nothing has to cross between parts.
All inputs are finite; a program needn't handle non-finite values.
Results may differ from the reference program's by a relative error of at most 0.0049.
Values may be sent and summed in bfloat16 or wider, within the bound.
No kernel may reach another device: no remote copies, remote signals or barrier semaphores. Data moves between devices by JAX's collectives and lax.ppermute only.
A program may use at most 64 MiB of HBM per device.

```python
import math
import jax
import jax.numpy as jnp
from jax import lax

HD = 128
H = 4
SEQ = 2048
N_CTX = 4


def draw_stick_offset(key, part):
    return jax.random.uniform(key, (H,), jnp.float32, -13.5, -7.0)


def block_scale(rng, extent, cuts, low, largest):
    gain, own = 1.0, jax.random.fold_in(rng, 6)
    for position, shards_of in cuts:
        heights = jnp.exp(jax.random.uniform(jax.random.fold_in(own, position), (shards_of,), jnp.float32, low / len(cuts), largest / len(cuts)))
        gain = gain * jnp.repeat(heights, extent[position] // shards_of).reshape([-1 if axis == position else 1 for axis in range(len(extent))])
    return gain


def gaussian(stream_key, dims, spread, reach, shards=(), kind=jnp.bfloat16):
    drawn = spread * jax.random.normal(stream_key, dims, jnp.float32)
    if shards:
        drawn = drawn * block_scale(stream_key, dims, shards, -0.22, 0.18)
    return jnp.clip(drawn, -reach, reach).astype(kind)


def setup_inputs(seed: int = 0, part: int = 0) -> dict:
    key_list = jax.random.split(jax.random.key(seed), 5)
    part_keys = jax.random.split(jax.random.fold_in(key_list[4], part), 5)
    return {
        "queries": gaussian(part_keys[0], (H, SEQ, HD), 3.0, 18.0, ((0, 4), (1, 4))),
        "keys": gaussian(part_keys[1], (H, SEQ, HD), 1.0, 6.0, ((0, 4), (1, 4))),
        "values": gaussian(part_keys[2], (H, SEQ, HD), 1.0, 6.0, ((0, 4), (1, 4))),
        "stick_offset": draw_stick_offset(jax.random.fold_in(key_list[4], 71), part),
    }


def reference(queries, keys, values, stick_offset):
    heads, seq, width = queries.shape
    rows = seq // N_CTX
    scale = 1.0 / math.sqrt(width)

    def one_head(items):
        qhead, khead, vhead, offset = items
        kblocks = khead.reshape(N_CTX, rows, width).astype(jnp.float32)
        vblocks = vhead.reshape(N_CTX, rows, width).astype(jnp.float32)
        kpos = jnp.arange(seq, dtype=jnp.int32).reshape(N_CTX, rows)

        def one_block(place):
            start = (place * rows).astype(jnp.int32)
            qrows = lax.dynamic_slice_in_dim(qhead, start, rows, 0).astype(jnp.float32)
            score = jnp.einsum('id,sjd->sij', qrows, kblocks) * scale + offset
            qpos = start + jnp.arange(rows, dtype=jnp.int32)
            live = kpos[:, None, :] < qpos[None, :, None]
            spent = jnp.where(live, jax.nn.softplus(score), 0.0)
            total = lax.optimization_barrier(jnp.sum(spent, axis=2))
            later = lax.cumsum(spent, axis=2, reverse=True) - spent
            weight = jnp.where(live, jnp.exp(jax.nn.log_sigmoid(score) - later), 0.0).astype(jnp.bfloat16)
            weight = lax.optimization_barrier(weight).astype(jnp.float32)
            partial_value = jnp.einsum('sij,sjd->sid', weight, vblocks)
            beyond = lax.cumsum(total, axis=0, reverse=True) - total
            return lax.optimization_barrier(jnp.sum(jnp.exp(-beyond)[:, :, None] * partial_value, axis=0)).astype(jnp.bfloat16)
        return lax.map(one_block, jnp.arange(N_CTX, dtype=jnp.int32)).reshape(seq, width)
    return lax.map(one_head, (queries, keys, values, stick_offset))
```

```python
import functools
import math

import jax
import jax.numpy as jnp
from jax import lax
from jax.experimental import pallas as pl
from jax.experimental.pallas import tpu as pltpu
from jax.sharding import PartitionSpec as P

ROW_TILE = 128


def pair_kernel(off_ref, q_ref, k_ref, v_ref, part_ref, tot_ref, *, diag, scale):
    tile = q_ref.shape[0]
    keys = k_ref.shape[0]
    score = (
        lax.dot_general(
            q_ref[...], k_ref[...], (((1,), (1,)), ((), ())), preferred_element_type=jnp.float32
        )
        * scale
        + off_ref[0]
    )
    soft = jnp.log1p(jnp.exp(-jnp.abs(score)))
    spent = jnp.maximum(score, 0.0) + soft
    logsig = jnp.minimum(score, 0.0) - soft
    if diag:
        row = pl.program_id(0) * tile + lax.broadcasted_iota(jnp.int32, (tile, keys), 0)
        col = lax.broadcasted_iota(jnp.int32, (tile, keys), 1)
        live = col < row
        spent = jnp.where(live, spent, 0.0)
    upper = (
        lax.broadcasted_iota(jnp.int32, (keys, keys), 0)
        > lax.broadcasted_iota(jnp.int32, (keys, keys), 1)
    ).astype(jnp.bfloat16)
    high = spent.astype(jnp.bfloat16)
    low = (spent - high.astype(jnp.float32)).astype(jnp.bfloat16)
    later = jnp.dot(high, upper, preferred_element_type=jnp.float32) + jnp.dot(
        low, upper, preferred_element_type=jnp.float32
    )
    weight = jnp.exp(logsig - later)
    if diag:
        weight = jnp.where(live, weight, 0.0)
    part_ref[...] = jnp.dot(
        weight.astype(jnp.bfloat16), v_ref[...], preferred_element_type=jnp.float32
    )
    tot_ref[...] = later[:, 0:1] + spent[:, 0:1]


def pair_terms(q, k, v, offset, diag):
    rows, width = q.shape
    keys = k.shape[0]
    tile = min(ROW_TILE, rows)
    kernel = functools.partial(pair_kernel, diag=diag, scale=1.0 / math.sqrt(width))
    flops = 2 * rows * keys * (2 * width + 2 * keys)
    part, tot = pl.pallas_call(
        kernel,
        grid=(rows // tile,),
        in_specs=[
            pl.BlockSpec(memory_space=pltpu.SMEM),
            pl.BlockSpec((tile, width), lambda r: (r, 0)),
            pl.BlockSpec((keys, width), lambda r: (0, 0)),
            pl.BlockSpec((keys, width), lambda r: (0, 0)),
        ],
        out_specs=[
            pl.BlockSpec((tile, width), lambda r: (r, 0)),
            pl.BlockSpec((tile, 1), lambda r: (r, 0)),
        ],
        out_shape=[
            jax.ShapeDtypeStruct((rows, width), jnp.float32),
            jax.ShapeDtypeStruct((rows, 1), jnp.float32),
        ],
        cost_estimate=pl.CostEstimate(
            flops=flops, transcendentals=3 * rows * keys, bytes_accessed=rows * width * 10
        ),
    )(offset.reshape(1), q, k, v)
    return part, tot


def one_head(q_own, k_own, v_own, offset):
    count = lax.axis_size("ctx")
    place = lax.axis_index("ctx")
    up = [(i, i + 1) for i in range(count - 1)]

    summed, spent_sum = pair_terms(q_own, k_own, v_own, offset, True)
    kv = (k_own, v_own)
    for step in range(1, count):
        kv = lax.ppermute(kv, "ctx", up)
        part, tot = pair_terms(q_own, kv[0], kv[1], offset, False)
        valid = place >= step
        summed = jnp.where(valid, summed + jnp.exp(-spent_sum) * part, summed)
        spent_sum = jnp.where(valid, spent_sum + tot, spent_sum)
    return summed.astype(jnp.bfloat16)


def on_device(queries, keys, values, stick_offset):
    results = [
        one_head(queries[h], keys[h], values[h], stick_offset[h]) for h in range(queries.shape[0])
    ]
    return jnp.stack(results, axis=0)


def solution(mesh):
    placed = (
        P(("head", "sub"), ("group", "ctx"), None),
        P(("head", "sub"), ("group", "ctx"), None),
        P(("head", "sub"), ("group", "ctx"), None),
        P(("head", "sub")),
    )
    return jax.shard_map(
        on_device,
        mesh=mesh,
        in_specs=placed,
        out_specs=P(("head", "sub"), ("group", "ctx"), None),
        check_vma=False,
    )
```

```python
import functools
import math

import jax
import jax.numpy as jnp
from jax import lax
from jax.experimental import pallas as pl
from jax.experimental.pallas import tpu as pltpu
from jax.sharding import PartitionSpec as P

ROW_TILE = 256


def pair_kernel(off_ref, q_ref, kv_ref, upper_ref, part_ref, tot_ref, *, diag, scale):
    tile = q_ref.shape[0]
    keys, width = kv_ref.shape[0], q_ref.shape[1]
    score = (
        lax.dot_general(
            q_ref[...],
            kv_ref[:, :width],
            (((1,), (1,)), ((), ())),
            preferred_element_type=jnp.float32,
        )
        * scale
        + off_ref[0]
    )
    soft = jnp.log1p(jnp.exp(-jnp.abs(score)))
    spent = jnp.maximum(score, 0.0) + soft
    logsig = jnp.minimum(score, 0.0) - soft
    if diag:
        row = pl.program_id(0) * tile + lax.broadcasted_iota(jnp.int32, (tile, keys), 0)
        col = lax.broadcasted_iota(jnp.int32, (tile, keys), 1)
        live = col < row
        spent = jnp.where(live, spent, 0.0)
    upper = upper_ref[...]
    high = spent.astype(jnp.bfloat16)
    low = (spent - high.astype(jnp.float32)).astype(jnp.bfloat16)
    later = jnp.dot(high, upper, preferred_element_type=jnp.float32) + jnp.dot(
        low, upper, preferred_element_type=jnp.float32
    )
    weight = jnp.exp(logsig - later)
    if diag:
        weight = jnp.where(live, weight, 0.0)
    part_ref[...] = jnp.dot(
        weight.astype(jnp.bfloat16), kv_ref[:, width:], preferred_element_type=jnp.float32
    )
    tot_ref[...] = later[:, 0:1] + spent[:, 0:1]


def pair_terms(q, kv, upper, offset, diag):
    rows, width = q.shape
    keys = kv.shape[0]
    tile = min(ROW_TILE, rows)
    kernel = functools.partial(pair_kernel, diag=diag, scale=1.0 / math.sqrt(width))
    flops = 2 * rows * keys * (2 * width + 2 * keys)
    part, tot = pl.pallas_call(
        kernel,
        grid=(rows // tile,),
        in_specs=[
            pl.BlockSpec(memory_space=pltpu.SMEM),
            pl.BlockSpec((tile, width), lambda r: (r, 0)),
            pl.BlockSpec((keys, 2 * width), lambda r: (0, 0)),
            pl.BlockSpec((keys, keys), lambda r: (0, 0)),
        ],
        out_specs=[
            pl.BlockSpec((tile, width), lambda r: (r, 0)),
            pl.BlockSpec((tile, 1), lambda r: (r, 0)),
        ],
        out_shape=[
            jax.ShapeDtypeStruct((rows, width), jnp.float32),
            jax.ShapeDtypeStruct((rows, 1), jnp.float32),
        ],
        cost_estimate=pl.CostEstimate(
            flops=flops, transcendentals=3 * rows * keys, bytes_accessed=rows * width * 10
        ),
    )(offset.reshape(1), q, kv, upper)
    return part, tot


def one_head(q_own, k_own, v_own, offset):
    count = lax.axis_size("ctx")
    place = lax.axis_index("ctx")
    up = [(i, i + 1) for i in range(count - 1)]

    keys = k_own.shape[0]
    upper = (
        lax.broadcasted_iota(jnp.int32, (keys, keys), 0)
        > lax.broadcasted_iota(jnp.int32, (keys, keys), 1)
    ).astype(jnp.bfloat16)
    kv = jnp.concatenate([k_own, v_own], axis=1)
    summed, spent_sum = pair_terms(q_own, kv, upper, offset, True)
    for step in range(1, count):
        kv = lax.ppermute(kv, "ctx", up)
        part, tot = pair_terms(q_own, kv, upper, offset, False)
        valid = place >= step
        summed = jnp.where(valid, summed + jnp.exp(-spent_sum) * part, summed)
        spent_sum = jnp.where(valid, spent_sum + tot, spent_sum)
    return summed.astype(jnp.bfloat16)


def on_device(queries, keys, values, stick_offset):
    results = [
        one_head(queries[h], keys[h], values[h], stick_offset[h]) for h in range(queries.shape[0])
    ]
    return jnp.stack(results, axis=0)


def solution(mesh):
    placed = (
        P(("head", "sub"), ("group", "ctx"), None),
        P(("head", "sub"), ("group", "ctx"), None),
        P(("head", "sub"), ("group", "ctx"), None),
        P(("head", "sub")),
    )
    return jax.shard_map(
        on_device,
        mesh=mesh,
        in_specs=placed,
        out_specs=P(("head", "sub"), ("group", "ctx"), None),
        check_vma=False,
    )
```

```python
import functools
import math

import jax
import numpy as np
import jax.numpy as jnp
from jax import lax
from jax.experimental import pallas as pl
from jax.experimental.pallas import tpu as pltpu
from jax.sharding import PartitionSpec as P


ROW_TILE = 256


def pair_kernel(scalar_ref, q_ref, kv_ref, upper_ref, *refs, diag, scale, last):
    if diag:
        summed_ref, spent_ref = refs
    else:
        in_summed_ref, in_spent_ref, summed_ref = refs[:3]
        spent_ref = None if last else refs[3]
    tile, _ = q_ref.shape
    keys = kv_ref.shape[0] // 2
    score = (
        lax.dot_general(
            q_ref[...],
            kv_ref[:keys, :],
            (((1,), (1,)), ((), ())),
            preferred_element_type=jnp.float32,
        )
        * scale
        + scalar_ref[0]
    )
    soft = jnp.log1p(jnp.exp(-jnp.abs(score)))
    spent = jnp.maximum(score, 0.0) + soft
    logsig = jnp.minimum(score, 0.0) - soft
    if diag:
        row = pl.program_id(0) * tile + lax.broadcasted_iota(jnp.int32, (tile, keys), 0)
        col = lax.broadcasted_iota(jnp.int32, (tile, keys), 1)
        live = col < row
        spent = jnp.where(live, spent, 0.0)
    upper = upper_ref[...]
    high = spent.astype(jnp.bfloat16)
    low = (spent - high.astype(jnp.float32)).astype(jnp.bfloat16)
    later = jnp.dot(high, upper, preferred_element_type=jnp.float32) + jnp.dot(
        low, upper, preferred_element_type=jnp.float32
    )
    weight = jnp.exp(logsig - later)
    if diag:
        weight = jnp.where(live, weight, 0.0)
    part = jnp.dot(weight.astype(jnp.bfloat16), kv_ref[keys:, :], preferred_element_type=jnp.float32)
    tot = later[:, 0:1] + spent[:, 0:1]
    if diag:
        summed_ref[...] = part
        spent_ref[...] = tot
        return
    use = scalar_ref[1] > 0.0
    before = in_spent_ref[...]
    summed = jnp.where(use, in_summed_ref[...] + jnp.exp(-before) * part, in_summed_ref[...])
    summed_ref[...] = summed.astype(summed_ref.dtype)
    if not last:
        spent_ref[...] = jnp.where(use, before + tot, before)


def pair_terms(q, kv, upper, scalars, carried=None, last=False):
    rows, width = q.shape
    keys = kv.shape[0] // 2
    tile = min(ROW_TILE, rows)
    diag = carried is None
    kernel = functools.partial(
        pair_kernel, diag=diag, scale=1.0 / math.sqrt(width), last=last
    )
    flops = 2 * rows * keys * (2 * width + 2 * keys)
    rows_spec = pl.BlockSpec((tile, width), lambda r: (r, 0))
    col_spec = pl.BlockSpec((tile, 1), lambda r: (r, 0))
    in_specs = [
        pl.BlockSpec(memory_space=pltpu.SMEM),
        rows_spec,
        pl.BlockSpec((2 * keys, width), lambda r: (0, 0)),
        pl.BlockSpec((keys, keys), lambda r: (0, 0)),
    ]
    args = [scalars, q, kv, upper]
    if not diag:
        in_specs += [rows_spec, col_spec]
        args += list(carried)
    out_specs = [rows_spec]
    out_shape = [jax.ShapeDtypeStruct((rows, width), jnp.bfloat16 if last else jnp.float32)]
    if not last:
        out_specs.append(col_spec)
        out_shape.append(jax.ShapeDtypeStruct((rows, 1), jnp.float32))
    return pl.pallas_call(
        kernel,
        grid=(rows // tile,),
        in_specs=in_specs,
        out_specs=out_specs,
        out_shape=out_shape,
        cost_estimate=pl.CostEstimate(
            flops=flops, transcendentals=3 * rows * keys, bytes_accessed=rows * width * 16
        ),
    )(*args)


def one_head(q_own, k_own, v_own, offset):
    count = lax.axis_size("ctx")
    place = lax.axis_index("ctx")
    route = [(i, (i + 1) % count) for i in range(count)]
    keys = k_own.shape[0]
    upper = jnp.asarray(np.triu(np.ones((keys, keys), np.float32), 1).T, jnp.bfloat16)
    kv = jnp.concatenate([k_own, v_own], axis=0)
    steps = jnp.arange(count, dtype=jnp.int32)
    table = jnp.stack(
        [jnp.broadcast_to(offset, (count,)), jnp.where(place >= steps, 1.0, 0.0)], axis=1
    ).astype(jnp.float32)
    carried = pair_terms(q_own, kv, upper, table[0])
    for step in range(1, count):
        kv = lax.ppermute(kv, "ctx", route)
        carried = pair_terms(
            q_own, kv, upper, table[step], carried, last=step == count - 1
        )
    if count == 1:
        return carried[0].astype(jnp.bfloat16)
    return carried[0]


def on_device(queries, keys, values, stick_offset):
    results = []
    for h in range(queries.shape[0]):
        results.append(one_head(queries[h], keys[h], values[h], stick_offset[h]))
    return jnp.stack(results, axis=0)


def solution(mesh):
    placed = (
        P(("head", "sub"), ("group", "ctx"), None),
        P(("head", "sub"), ("group", "ctx"), None),
        P(("head", "sub"), ("group", "ctx"), None),
        P(("head", "sub")),
    )
    return jax.shard_map(
        on_device,
        mesh=mesh,
        in_specs=placed,
        out_specs=P(("head", "sub"), ("group", "ctx"), None),
        check_vma=False,
    )
```

```python
import functools
import math

import jax
import numpy as np
import jax.numpy as jnp
from jax import lax
from jax.experimental import pallas as pl
from jax.experimental.pallas import tpu as pltpu
from jax.sharding import PartitionSpec as P


ROW_TILE = 256
LOG2E = 1.4426950408889634
LN2 = 0.6931471805599453


def pair_kernel(scalar_ref, q_ref, kv_ref, upper_ref, *refs, diag, scale, last):
    if diag:
        summed_ref, spent_ref = refs
    else:
        in_summed_ref, in_spent_ref, summed_ref = refs[:3]
        spent_ref = None if last else refs[3]
    tile, _ = q_ref.shape
    keys = kv_ref.shape[0] // 2
    score = (
        lax.dot_general(
            q_ref[...],
            kv_ref[:keys, :],
            (((1,), (1,)), ((), ())),
            preferred_element_type=jnp.float32,
        )
        * (scale * LOG2E)
        + scalar_ref[0] * LOG2E
    )
    spent = jnp.maximum(score, 0.0) + jnp.log2(1.0 + jnp.exp2(-jnp.abs(score)))
    if diag:
        row = pl.program_id(0) * tile + lax.broadcasted_iota(jnp.int32, (tile, keys), 0)
        col = lax.broadcasted_iota(jnp.int32, (tile, keys), 1)
        live = col < row
        spent = jnp.where(live, spent, 0.0)
    upper = upper_ref[...]
    high = spent.astype(jnp.bfloat16)
    low = (spent - high.astype(jnp.float32)).astype(jnp.bfloat16)
    later = jnp.dot(high, upper, preferred_element_type=jnp.float32) + jnp.dot(
        low, upper, preferred_element_type=jnp.float32
    )
    weight = jnp.exp2((score - spent) - later)
    if diag:
        weight = jnp.where(live, weight, 0.0)
    part = jnp.dot(weight.astype(jnp.bfloat16), kv_ref[keys:, :], preferred_element_type=jnp.float32)
    tot = (later[:, 0:1] + spent[:, 0:1]) * LN2
    if diag:
        summed_ref[...] = part
        spent_ref[...] = tot
        return
    use = scalar_ref[1] > 0.0
    before = in_spent_ref[...]
    summed = jnp.where(use, in_summed_ref[...] + jnp.exp(-before) * part, in_summed_ref[...])
    summed_ref[...] = summed.astype(summed_ref.dtype)
    if not last:
        spent_ref[...] = jnp.where(use, before + tot, before)


def stack_kernel(k_ref, v_ref, out_ref):
    rows = k_ref.shape[0]
    out_ref[:rows, :] = k_ref[...]
    out_ref[rows:, :] = v_ref[...]


def stacked(k, v):
    rows, width = k.shape
    whole = pl.BlockSpec(memory_space=pltpu.VMEM)
    return pl.pallas_call(
        stack_kernel,
        in_specs=[whole, whole],
        out_specs=whole,
        out_shape=jax.ShapeDtypeStruct((2 * rows, width), k.dtype),
    )(k, v)


def pair_terms(q, kv, upper, scalars, carried=None, last=False):
    rows, width = q.shape
    keys = kv.shape[0] // 2
    tile = min(ROW_TILE, rows)
    diag = carried is None
    kernel = functools.partial(
        pair_kernel, diag=diag, scale=1.0 / math.sqrt(width), last=last
    )
    flops = 2 * rows * keys * (2 * width + 2 * keys)
    rows_spec = pl.BlockSpec((tile, width), lambda r: (r, 0))
    col_spec = pl.BlockSpec((tile, 1), lambda r: (r, 0))
    in_specs = [
        pl.BlockSpec(memory_space=pltpu.SMEM),
        rows_spec,
        pl.BlockSpec(memory_space=pltpu.VMEM),
        pl.BlockSpec((keys, keys), lambda r: (0, 0)),
    ]
    args = [scalars, q, kv, upper]
    if not diag:
        in_specs += [rows_spec, col_spec]
        args += list(carried)
    out_specs = [rows_spec]
    out_shape = [jax.ShapeDtypeStruct((rows, width), jnp.bfloat16 if last else jnp.float32)]
    if not last:
        out_specs.append(col_spec)
        out_shape.append(jax.ShapeDtypeStruct((rows, 1), jnp.float32))
    return pl.pallas_call(
        kernel,
        grid=(rows // tile,),
        in_specs=in_specs,
        out_specs=out_specs,
        out_shape=out_shape,
        cost_estimate=pl.CostEstimate(
            flops=flops, transcendentals=3 * rows * keys, bytes_accessed=rows * width * 16
        ),
    )(*args)


def one_head(q_own, k_own, v_own, offset):
    count = lax.axis_size("ctx")
    place = lax.axis_index("ctx")
    route = [(i, (i + 1) % count) for i in range(count)]
    keys = k_own.shape[0]
    upper = jnp.asarray(np.triu(np.ones((keys, keys), np.float32), 1).T, jnp.bfloat16)
    kv = stacked(k_own, v_own)
    steps = jnp.arange(count, dtype=jnp.int32)
    table = jnp.stack(
        [jnp.broadcast_to(offset, (count,)), jnp.where(place >= steps, 1.0, 0.0)], axis=1
    ).astype(jnp.float32)
    carried = pair_terms(q_own, kv, upper, table[0])
    for step in range(1, count):
        kv = lax.ppermute(kv, "ctx", route)
        carried = pair_terms(
            q_own, kv, upper, table[step], carried, last=step == count - 1
        )
    if count == 1:
        return carried[0].astype(jnp.bfloat16)
    return carried[0]


def on_device(queries, keys, values, stick_offset):
    results = []
    for h in range(queries.shape[0]):
        results.append(one_head(queries[h], keys[h], values[h], stick_offset[h]))
    return jnp.stack(results, axis=0)


def solution(mesh):
    placed = (
        P(("head", "sub"), ("group", "ctx"), None),
        P(("head", "sub"), ("group", "ctx"), None),
        P(("head", "sub"), ("group", "ctx"), None),
        P(("head", "sub")),
    )
    return jax.shard_map(
        on_device,
        mesh=mesh,
        in_specs=placed,
        out_specs=P(("head", "sub"), ("group", "ctx"), None),
        check_vma=False,
    )
```

```python
import functools
import math

import jax
import numpy as np
import jax.numpy as jnp
from jax import lax
from jax.experimental import pallas as pl
from jax.experimental.pallas import tpu as pltpu
from jax.sharding import PartitionSpec as P


ROW_TILE = 256
LOG2E = 1.4426950408889634
LN2 = 0.6931471805599453


def pair_kernel(scalar_ref, q_ref, kv_ref, upper_ref, *refs, mode, scale):
    diag = mode == "diag"
    if mode == "step":
        in_summed_ref, in_spent_ref, summed_ref, spent_ref = refs
    else:
        summed_ref = refs[0]
    tile, _ = q_ref.shape
    keys = kv_ref.shape[0] // 2
    score = (
        lax.dot_general(
            q_ref[...],
            kv_ref[:keys, :],
            (((1,), (1,)), ((), ())),
            preferred_element_type=jnp.float32,
        )
        * (scale * LOG2E)
        + scalar_ref[0] * LOG2E
    )
    spent = jnp.maximum(score, 0.0) + jnp.log2(1.0 + jnp.exp2(-jnp.abs(score)))
    if diag:
        row = pl.program_id(0) * tile + lax.broadcasted_iota(jnp.int32, (tile, keys), 0)
        col = lax.broadcasted_iota(jnp.int32, (tile, keys), 1)
        live = col < row
        spent = jnp.where(live, spent, 0.0)
    upper = upper_ref[...]
    high = spent.astype(jnp.bfloat16)
    low = (spent - high.astype(jnp.float32)).astype(jnp.bfloat16)
    later = jnp.dot(high, upper, preferred_element_type=jnp.float32) + jnp.dot(
        low, upper, preferred_element_type=jnp.float32
    )
    weight = jnp.exp2((score - spent) - later)
    if diag:
        weight = jnp.where(live, weight, 0.0)
    part = jnp.dot(weight.astype(jnp.bfloat16), kv_ref[keys:, :], preferred_element_type=jnp.float32)
    if mode == "far":
        summed_ref[...] = part.astype(summed_ref.dtype)
        return
    tot = (later[:, 0:1] + spent[:, 0:1]) * LN2
    if diag:
        summed_ref[...] = part
        refs[1][...] = tot
        return
    use = scalar_ref[1] > 0.0
    before = in_spent_ref[...]
    summed_ref[...] = jnp.where(use, in_summed_ref[...] + jnp.exp(-before) * part, in_summed_ref[...])
    spent_ref[...] = jnp.where(use, before + tot, before)


def pair_terms(q, kv, upper, scalars, carried=None, mode="step"):
    rows, width = q.shape
    keys = kv.shape[0] // 2
    tile = min(ROW_TILE, rows)
    kernel = functools.partial(pair_kernel, mode=mode, scale=1.0 / math.sqrt(width))
    flops = 2 * rows * keys * (2 * width + 2 * keys)
    rows_spec = pl.BlockSpec((tile, width), lambda r: (r, 0))
    col_spec = pl.BlockSpec((tile, 1), lambda r: (r, 0))
    in_specs = [
        pl.BlockSpec(memory_space=pltpu.SMEM),
        rows_spec,
        pl.BlockSpec(memory_space=pltpu.VMEM),
        pl.BlockSpec((keys, keys), lambda r: (0, 0)),
    ]
    args = [scalars, q, kv, upper]
    if mode == "step":
        in_specs += [rows_spec, col_spec]
        args += list(carried)
    out_specs = [rows_spec]
    out_shape = [jax.ShapeDtypeStruct((rows, width), jnp.bfloat16 if mode == "far" else jnp.float32)]
    if mode != "far":
        out_specs.append(col_spec)
        out_shape.append(jax.ShapeDtypeStruct((rows, 1), jnp.float32))
    return pl.pallas_call(
        kernel,
        grid=(rows // tile,),
        in_specs=in_specs,
        out_specs=out_specs,
        out_shape=out_shape,
        cost_estimate=pl.CostEstimate(
            flops=flops, transcendentals=3 * rows * keys, bytes_accessed=rows * width * 16
        ),
    )(*args)


def one_head(q_own, k_own, v_own, offset):
    count = lax.axis_size("ctx")
    place = lax.axis_index("ctx")
    up = [(i, i + 1) for i in range(count - 1)]
    down = [(i, i - 1) for i in range(1, count)]
    keys = k_own.shape[0]
    upper = jnp.asarray(np.triu(np.ones((keys, keys), np.float32), 1).T, jnp.bfloat16)
    kv = jnp.concatenate([k_own, v_own], axis=0)
    steps = jnp.arange(count, dtype=jnp.int32)
    table = jnp.stack(
        [jnp.broadcast_to(offset, (count,)), jnp.where(place >= steps, 1.0, 0.0)], axis=1
    ).astype(jnp.float32)
    summed, spent = pair_terms(q_own, kv, upper, table[0], mode="diag")
    if count == 1:
        return summed.astype(jnp.bfloat16)
    for step in range(1, count - 1):
        kv = lax.ppermute(kv, "ctx", up)
        if step == 1:
            q_next = lax.ppermute(q_own, "ctx", down)
        if step < count - 2:
            summed, spent = pair_terms(q_own, kv, upper, table[step], (summed, spent))
    if count == 2:
        q_next = lax.ppermute(q_own, "ctx", down)
    far = pair_terms(q_next, kv, upper, table[0], mode="far")[0]
    far = lax.ppermute(far, "ctx", up)
    if count > 2:
        summed, spent = pair_terms(
            q_own, kv, upper, table[count - 2], (summed, spent)
        )
    out = jnp.where(
        place == count - 1, summed + jnp.exp(-spent) * far.astype(jnp.float32), summed
    )
    return out.astype(jnp.bfloat16)


def on_device(queries, keys, values, stick_offset):
    results = []
    for h in range(queries.shape[0]):
        results.append(one_head(queries[h], keys[h], values[h], stick_offset[h]))
    return jnp.stack(results, axis=0)


def solution(mesh):
    placed = (
        P(("head", "sub"), ("group", "ctx"), None),
        P(("head", "sub"), ("group", "ctx"), None),
        P(("head", "sub"), ("group", "ctx"), None),
        P(("head", "sub")),
    )
    return jax.shard_map(
        on_device,
        mesh=mesh,
        in_specs=placed,
        out_specs=P(("head", "sub"), ("group", "ctx"), None),
        check_vma=False,
    )
```

```python
import functools
import math

import jax
import numpy as np
import jax.numpy as jnp
from jax import lax
from jax.experimental import pallas as pl
from jax.experimental.pallas import tpu as pltpu
from jax.sharding import PartitionSpec as P


ROW_TILE = 256
LOG2E = 1.4426950408889634
LN2 = 0.6931471805599453


def pair_kernel(scalar_ref, q_ref, kv_ref, upper_ref, *refs, mode, scale):
    diag = mode == "diag"
    if mode == "step":
        in_summed_ref, in_spent_ref, summed_ref, spent_ref = refs
    else:
        summed_ref = refs[0]
    tile, _ = q_ref.shape
    keys = kv_ref.shape[0] // 2
    score = (
        lax.dot_general(
            q_ref[...],
            kv_ref[:keys, :],
            (((1,), (1,)), ((), ())),
            preferred_element_type=jnp.float32,
        )
        * (scale * LOG2E)
        + scalar_ref[0] * LOG2E
    )
    spent = jnp.maximum(score, 0.0) + jnp.log2(1.0 + jnp.exp2(-jnp.abs(score)))
    if diag:
        row = pl.program_id(0) * tile + lax.broadcasted_iota(jnp.int32, (tile, keys), 0)
        col = lax.broadcasted_iota(jnp.int32, (tile, keys), 1)
        live = col < row
        spent = jnp.where(live, spent, 0.0)
    upper = upper_ref[...]
    high = spent.astype(jnp.bfloat16)
    low = (spent - high.astype(jnp.float32)).astype(jnp.bfloat16)
    later = jnp.dot(high, upper, preferred_element_type=jnp.float32) + jnp.dot(
        low, upper, preferred_element_type=jnp.float32
    )
    weight = jnp.exp2((score - spent) - later)
    if diag:
        weight = jnp.where(live, weight, 0.0)
    part = jnp.dot(weight.astype(jnp.bfloat16), kv_ref[keys:, :], preferred_element_type=jnp.float32)
    if mode == "far":
        summed_ref[...] = part.astype(summed_ref.dtype)
        return
    tot = (later[:, 0:1] + spent[:, 0:1]) * LN2
    if diag:
        summed_ref[...] = part
        refs[1][...] = tot
        return
    use = scalar_ref[1] > 0.0
    before = in_spent_ref[...]
    summed_ref[...] = jnp.where(use, in_summed_ref[...] + jnp.exp(-before) * part, in_summed_ref[...])
    spent_ref[...] = jnp.where(use, before + tot, before)


def pair_terms(q, kv, upper, scalars, carried=None, mode="step"):
    rows, width = q.shape
    keys = kv.shape[0] // 2
    tile = min(ROW_TILE, rows)
    kernel = functools.partial(pair_kernel, mode=mode, scale=1.0 / math.sqrt(width))
    flops = 2 * rows * keys * (2 * width + 2 * keys)
    rows_spec = pl.BlockSpec((tile, width), lambda r: (r, 0))
    col_spec = pl.BlockSpec((tile, 1), lambda r: (r, 0))
    in_specs = [
        pl.BlockSpec(memory_space=pltpu.SMEM),
        rows_spec,
        pl.BlockSpec(memory_space=pltpu.VMEM),
        pl.BlockSpec((keys, keys), lambda r: (0, 0)),
    ]
    args = [scalars, q, kv, upper]
    if mode == "step":
        in_specs += [rows_spec, col_spec]
        args += list(carried)
    out_specs = [rows_spec]
    out_shape = [jax.ShapeDtypeStruct((rows, width), jnp.bfloat16 if mode == "far" else jnp.float32)]
    if mode != "far":
        out_specs.append(col_spec)
        out_shape.append(jax.ShapeDtypeStruct((rows, 1), jnp.float32))
    return pl.pallas_call(
        kernel,
        grid=(rows // tile,),
        in_specs=in_specs,
        out_specs=out_specs,
        out_shape=out_shape,
        cost_estimate=pl.CostEstimate(
            flops=flops, transcendentals=3 * rows * keys, bytes_accessed=rows * width * 16
        ),
    )(*args)


def one_head(q_own, k_own, v_own, offset):
    count = lax.axis_size("ctx")
    place = lax.axis_index("ctx")
    up = [(i, (i + 1) % count) for i in range(count)]
    down = [(i, (i - 1) % count) for i in range(count)]
    rows = q_own.shape[0]
    keys = k_own.shape[0]
    upper = jnp.asarray(np.triu(np.ones((keys, keys), np.float32), 1).T, jnp.bfloat16)
    own_kv = jnp.concatenate([k_own, v_own], axis=0)
    steps = jnp.arange(count, dtype=jnp.int32)
    table = jnp.stack(
        [jnp.broadcast_to(offset, (count,)), jnp.where(place >= steps, 1.0, 0.0)], axis=1
    ).astype(jnp.float32)
    summed, spent = pair_terms(q_own, own_kv, upper, table[0], mode="diag")
    if count == 1:
        return summed.astype(jnp.bfloat16)
    if count == 2:
        kv = lax.ppermute(own_kv, "ctx", up)
        summed, spent = pair_terms(q_own, kv, upper, table[1], (summed, spent))
        return summed.astype(jnp.bfloat16)
    last = place == count - 1
    sent = jnp.concatenate([jnp.where(last, q_own, k_own), v_own], axis=0)
    kv = lax.ppermute(sent, "ctx", up)
    far = pair_terms(kv[:rows], own_kv, upper, table[0], mode="far")[0]
    for step in range(1, count - 1):
        if step > 1:
            kv = lax.ppermute(kv, "ctx", up)
        if step < count - 2:
            summed, spent = pair_terms(q_own, kv, upper, table[step], (summed, spent))
    far = lax.ppermute(far, "ctx", down)
    summed, spent = pair_terms(q_own, kv, upper, table[count - 2], (summed, spent))
    out = jnp.where(last, summed + jnp.exp(-spent) * far.astype(jnp.float32), summed)
    return out.astype(jnp.bfloat16)


def on_device(queries, keys, values, stick_offset):
    results = []
    for h in range(queries.shape[0]):
        results.append(one_head(queries[h], keys[h], values[h], stick_offset[h]))
    return jnp.stack(results, axis=0)


def solution(mesh):
    placed = (
        P(("head", "sub"), ("group", "ctx"), None),
        P(("head", "sub"), ("group", "ctx"), None),
        P(("head", "sub"), ("group", "ctx"), None),
        P(("head", "sub")),
    )
    return jax.shard_map(
        on_device,
        mesh=mesh,
        in_specs=placed,
        out_specs=P(("head", "sub"), ("group", "ctx"), None),
        check_vma=False,
    )
```

```python
import functools
import math

import jax
import numpy as np
import jax.numpy as jnp
from jax import lax
from jax.experimental import pallas as pl
from jax.experimental.pallas import tpu as pltpu
from jax.sharding import PartitionSpec as P


ROW_TILE = 256
LOG2E = 1.4426950408889634
LN2 = 0.6931471805599453


def pair_kernel(scalar_ref, q_ref, kv_ref, upper_ref, *refs, mode, scale):
    diag = mode == "diag"
    if mode in ("step", "final"):
        in_summed_ref, in_spent_ref, summed_ref, spent_ref = refs
    else:
        summed_ref = refs[0]
    tile, _ = q_ref.shape
    keys = kv_ref.shape[0] // 2
    score = (
        lax.dot_general(
            q_ref[...],
            kv_ref[:keys, :],
            (((1,), (1,)), ((), ())),
            preferred_element_type=jnp.float32,
        )
        * (scale * LOG2E)
        + scalar_ref[0] * LOG2E
    )
    spent = jnp.maximum(score, 0.0) + jnp.log2(1.0 + jnp.exp2(-jnp.abs(score)))
    if diag:
        row = pl.program_id(0) * tile + lax.broadcasted_iota(jnp.int32, (tile, keys), 0)
        col = lax.broadcasted_iota(jnp.int32, (tile, keys), 1)
        live = col < row
        spent = jnp.where(live, spent, 0.0)
    upper = upper_ref[...]
    high = spent.astype(jnp.bfloat16)
    low = (spent - high.astype(jnp.float32)).astype(jnp.bfloat16)
    later = jnp.dot(high, upper, preferred_element_type=jnp.float32) + jnp.dot(
        low, upper, preferred_element_type=jnp.float32
    )
    weight = jnp.exp2((score - spent) - later)
    if diag:
        weight = jnp.where(live, weight, 0.0)
    part = jnp.dot(weight.astype(jnp.bfloat16), kv_ref[keys:, :], preferred_element_type=jnp.float32)
    if mode == "far":
        summed_ref[...] = part.astype(summed_ref.dtype)
        return
    tot = (later[:, 0:1] + spent[:, 0:1]) * LN2
    if diag:
        summed_ref[...] = part
        refs[1][...] = tot
        return
    use = scalar_ref[1] > 0.0
    before = in_spent_ref[...]
    summed_ref[...] = jnp.where(use, in_summed_ref[...] + jnp.exp(-before) * part, in_summed_ref[...])
    after = jnp.where(use, before + tot, before)
    if mode == "final":
        spent_ref[...] = jnp.broadcast_to(jnp.exp(-after), spent_ref.shape)
    else:
        spent_ref[...] = after


def payload_kernel(flag_ref, q_ref, k_ref, v_ref, own_ref, sent_ref):
    rows = k_ref.shape[0]
    own_ref[:rows, :] = k_ref[...]
    own_ref[rows:, :] = v_ref[...]
    sent_ref[rows:, :] = v_ref[...]

    @pl.when(flag_ref[0] > 0.0)
    def _():
        sent_ref[:rows, :] = q_ref[...]

    @pl.when(flag_ref[0] <= 0.0)
    def _():
        sent_ref[:rows, :] = k_ref[...]


def payloads(flag, q, k, v):
    rows, width = k.shape
    block = pl.BlockSpec((rows, width), lambda i: (0, 0))
    both = pl.BlockSpec((2 * rows, width), lambda i: (0, 0))
    shape = jax.ShapeDtypeStruct((2 * rows, width), k.dtype)
    return pl.pallas_call(
        payload_kernel,
        grid=(1,),
        in_specs=[pl.BlockSpec(memory_space=pltpu.SMEM), block, block, block],
        out_specs=[both, both],
        out_shape=[shape, shape],
    )(flag, q, k, v)


def pair_terms(q, kv, upper, scalars, carried=None, mode="step", rows=None):
    width = q.shape[1]
    rows = q.shape[0] if rows is None else rows
    keys = kv.shape[0] // 2
    tile = min(ROW_TILE, rows)
    kernel = functools.partial(pair_kernel, mode=mode, scale=1.0 / math.sqrt(width))
    flops = 2 * rows * keys * (2 * width + 2 * keys)
    rows_spec = pl.BlockSpec((tile, width), lambda r: (r, 0))
    col_spec = pl.BlockSpec((tile, 1), lambda r: (r, 0))
    in_specs = [
        pl.BlockSpec(memory_space=pltpu.SMEM),
        rows_spec,
        pl.BlockSpec(memory_space=pltpu.VMEM),
        pl.BlockSpec(memory_space=pltpu.VMEM),
    ]
    args = [scalars, q, kv, upper]
    if mode in ("step", "final"):
        in_specs += [rows_spec, col_spec]
        args += list(carried)
    out_specs = [rows_spec]
    out_shape = [jax.ShapeDtypeStruct((rows, width), jnp.bfloat16 if mode == "far" else jnp.float32)]
    if mode == "final":
        out_specs.append(rows_spec)
        out_shape.append(jax.ShapeDtypeStruct((rows, width), jnp.float32))
    elif mode != "far":
        out_specs.append(col_spec)
        out_shape.append(jax.ShapeDtypeStruct((rows, 1), jnp.float32))
    return pl.pallas_call(
        kernel,
        grid=(rows // tile,),
        in_specs=in_specs,
        out_specs=out_specs,
        out_shape=out_shape,
        cost_estimate=pl.CostEstimate(
            flops=flops, transcendentals=3 * rows * keys, bytes_accessed=rows * width * 16
        ),
    )(*args)


def one_head(q_own, k_own, v_own, offset):
    count = lax.axis_size("ctx")
    place = lax.axis_index("ctx")
    up = [(i, (i + 1) % count) for i in range(count)]
    down = [(i, (i - 1) % count) for i in range(count)]
    rows = q_own.shape[0]
    keys = k_own.shape[0]
    upper = jnp.asarray(np.triu(np.ones((keys, keys), np.float32), 1).T, jnp.bfloat16)
    steps = jnp.arange(count, dtype=jnp.int32)
    table = jnp.stack(
        [jnp.broadcast_to(offset, (count,)), jnp.where(place >= steps, 1.0, 0.0)], axis=1
    ).astype(jnp.float32)
    last = place == count - 1
    own_kv, sent = payloads(jnp.where(last, 1.0, 0.0).reshape(1), q_own, k_own, v_own)
    summed, spent = pair_terms(q_own, own_kv, upper, table[0], mode="diag")
    if count == 1:
        return summed.astype(jnp.bfloat16)
    if count == 2:
        kv = lax.ppermute(own_kv, "ctx", up)
        summed, spent = pair_terms(q_own, kv, upper, table[1], (summed, spent))
        return summed.astype(jnp.bfloat16)
    kv = lax.ppermute(sent, "ctx", up)
    far = pair_terms(kv, own_kv, upper, table[0], mode="far", rows=rows)[0]
    for step in range(1, count - 1):
        if step > 1:
            kv = lax.ppermute(kv, "ctx", up)
        if step < count - 2:
            summed, spent = pair_terms(q_own, kv, upper, table[step], (summed, spent))
    far = lax.ppermute(far, "ctx", down)
    summed, scale = pair_terms(q_own, kv, upper, table[count - 2], (summed, spent), mode="final")
    out = jnp.where(last, summed + scale * far.astype(jnp.float32), summed)
    return out.astype(jnp.bfloat16)


def on_device(queries, keys, values, stick_offset):
    results = []
    for h in range(queries.shape[0]):
        results.append(one_head(queries[h], keys[h], values[h], stick_offset[h]))
    return jnp.stack(results, axis=0)


def solution(mesh):
    placed = (
        P(("head", "sub"), ("group", "ctx"), None),
        P(("head", "sub"), ("group", "ctx"), None),
        P(("head", "sub"), ("group", "ctx"), None),
        P(("head", "sub")),
    )
    return jax.shard_map(
        on_device,
        mesh=mesh,
        in_specs=placed,
        out_specs=P(("head", "sub"), ("group", "ctx"), None),
        check_vma=False,
    )
```

```python
import functools
import math

import jax
import numpy as np
import jax.numpy as jnp
from jax import lax
from jax.experimental import pallas as pl
from jax.experimental.pallas import tpu as pltpu
from jax.sharding import PartitionSpec as P


ROW_TILE = 256
LOG2E = 1.4426950408889634
LN2 = 0.6931471805599453


def pair_kernel(scalar_ref, q_ref, kv_ref, upper_ref, *refs, mode, scale, rows, tile):
    for r in range(rows // tile):
        pair_rows(scalar_ref, q_ref, kv_ref, upper_ref, refs, mode, scale, r, tile)


def pair_rows(scalar_ref, q_all, kv_ref, upper_ref, refs, mode, scale, r, tile):
    diag = mode == "diag"
    rs = slice(r * tile, (r + 1) * tile)
    if mode in ("step", "final"):
        in_summed_ref, in_spent_ref, summed_ref, spent_ref = (ref.at[rs] for ref in refs)
    else:
        summed_ref = refs[0].at[rs]
    q_ref = q_all.at[rs]
    keys = kv_ref.shape[0] // 2
    score = (
        lax.dot_general(
            q_ref[...],
            kv_ref[:keys, :],
            (((1,), (1,)), ((), ())),
            preferred_element_type=jnp.float32,
        )
        * (scale * LOG2E)
        + scalar_ref[0] * LOG2E
    )
    spent = jnp.maximum(score, 0.0) + jnp.log2(1.0 + jnp.exp2(-jnp.abs(score)))
    if diag:
        row = r * tile + lax.broadcasted_iota(jnp.int32, (tile, keys), 0)
        col = lax.broadcasted_iota(jnp.int32, (tile, keys), 1)
        live = col < row
        spent = jnp.where(live, spent, 0.0)
    upper = upper_ref[...]
    high = spent.astype(jnp.bfloat16)
    low = (spent - high.astype(jnp.float32)).astype(jnp.bfloat16)
    later = jnp.dot(high, upper, preferred_element_type=jnp.float32) + jnp.dot(
        low, upper, preferred_element_type=jnp.float32
    )
    weight = jnp.exp2((score - spent) - later)
    if diag:
        weight = jnp.where(live, weight, 0.0)
    part = jnp.dot(weight.astype(jnp.bfloat16), kv_ref[keys:, :], preferred_element_type=jnp.float32)
    if mode == "far":
        summed_ref[...] = part.astype(summed_ref.dtype)
        return
    tot = (later[:, 0:1] + spent[:, 0:1]) * LN2
    if diag:
        summed_ref[...] = part
        refs[1].at[rs][...] = tot
        return
    use = scalar_ref[1] > 0.0
    before = in_spent_ref[...]
    summed_ref[...] = jnp.where(use, in_summed_ref[...] + jnp.exp(-before) * part, in_summed_ref[...])
    after = jnp.where(use, before + tot, before)
    if mode == "final":
        spent_ref[...] = jnp.broadcast_to(jnp.exp(-after), spent_ref.shape)
    else:
        spent_ref[...] = after


def payload_kernel(flag_ref, q_ref, k_ref, v_ref, own_ref, sent_ref):
    rows = k_ref.shape[0]
    own_ref[:rows, :] = k_ref[...]
    own_ref[rows:, :] = v_ref[...]
    sent_ref[rows:, :] = v_ref[...]

    @pl.when(flag_ref[0] > 0.0)
    def _():
        sent_ref[:rows, :] = q_ref[...]

    @pl.when(flag_ref[0] <= 0.0)
    def _():
        sent_ref[:rows, :] = k_ref[...]


def payloads(flag, q, k, v):
    rows, width = k.shape
    block = pl.BlockSpec((rows, width), lambda i: (0, 0))
    both = pl.BlockSpec((2 * rows, width), lambda i: (0, 0))
    shape = jax.ShapeDtypeStruct((2 * rows, width), k.dtype)
    return pl.pallas_call(
        payload_kernel,
        grid=(1,),
        in_specs=[pl.BlockSpec(memory_space=pltpu.SMEM), block, block, block],
        out_specs=[both, both],
        out_shape=[shape, shape],
    )(flag, q, k, v)


def pair_terms(q, kv, upper, scalars, carried=None, mode="step", rows=None):
    width = q.shape[1]
    rows = q.shape[0] if rows is None else rows
    keys = kv.shape[0] // 2
    tile = min(ROW_TILE, rows)
    kernel = functools.partial(
        pair_kernel, mode=mode, scale=1.0 / math.sqrt(width), rows=rows, tile=tile
    )
    flops = 2 * rows * keys * (2 * width + 2 * keys)
    vmem = pl.BlockSpec(memory_space=pltpu.VMEM)
    in_specs = [pl.BlockSpec(memory_space=pltpu.SMEM), vmem, vmem, vmem]
    args = [scalars, q, kv, upper]
    if mode in ("step", "final"):
        in_specs += [vmem, vmem]
        args += list(carried)
    out_specs = [vmem]
    out_shape = [jax.ShapeDtypeStruct((rows, width), jnp.bfloat16 if mode == "far" else jnp.float32)]
    if mode == "final":
        out_specs.append(vmem)
        out_shape.append(jax.ShapeDtypeStruct((rows, width), jnp.float32))
    elif mode != "far":
        out_specs.append(vmem)
        out_shape.append(jax.ShapeDtypeStruct((rows, 1), jnp.float32))
    return pl.pallas_call(
        kernel,
        in_specs=in_specs,
        out_specs=out_specs,
        out_shape=out_shape,
        cost_estimate=pl.CostEstimate(
            flops=flops, transcendentals=3 * rows * keys, bytes_accessed=rows * width * 16
        ),
    )(*args)


def one_head(q_own, k_own, v_own, offset):
    count = lax.axis_size("ctx")
    place = lax.axis_index("ctx")
    up = [(i, (i + 1) % count) for i in range(count)]
    down = [(i, (i - 1) % count) for i in range(count)]
    rows = q_own.shape[0]
    keys = k_own.shape[0]
    upper = jnp.asarray(np.triu(np.ones((keys, keys), np.float32), 1).T, jnp.bfloat16)
    steps = jnp.arange(count, dtype=jnp.int32)
    table = jnp.stack(
        [jnp.broadcast_to(offset, (count,)), jnp.where(place >= steps, 1.0, 0.0)], axis=1
    ).astype(jnp.float32)
    last = place == count - 1
    own_kv, sent = payloads(jnp.where(last, 1.0, 0.0).reshape(1), q_own, k_own, v_own)
    summed, spent = pair_terms(q_own, own_kv, upper, table[0], mode="diag")
    if count == 1:
        return summed.astype(jnp.bfloat16)
    if count == 2:
        kv = lax.ppermute(own_kv, "ctx", up)
        summed, spent = pair_terms(q_own, kv, upper, table[1], (summed, spent))
        return summed.astype(jnp.bfloat16)
    kv = lax.ppermute(sent, "ctx", up)
    far = pair_terms(kv, own_kv, upper, table[0], mode="far", rows=rows)[0]
    for step in range(1, count - 1):
        if step > 1:
            kv = lax.ppermute(kv, "ctx", up)
        if step < count - 2:
            summed, spent = pair_terms(q_own, kv, upper, table[step], (summed, spent))
    far = lax.ppermute(far, "ctx", down)
    summed, scale = pair_terms(q_own, kv, upper, table[count - 2], (summed, spent), mode="final")
    out = jnp.where(last, summed + scale * far.astype(jnp.float32), summed)
    return out.astype(jnp.bfloat16)


def on_device(queries, keys, values, stick_offset):
    results = []
    for h in range(queries.shape[0]):
        results.append(one_head(queries[h], keys[h], values[h], stick_offset[h]))
    return jnp.stack(results, axis=0)


def solution(mesh):
    placed = (
        P(("head", "sub"), ("group", "ctx"), None),
        P(("head", "sub"), ("group", "ctx"), None),
        P(("head", "sub"), ("group", "ctx"), None),
        P(("head", "sub")),
    )
    return jax.shard_map(
        on_device,
        mesh=mesh,
        in_specs=placed,
        out_specs=P(("head", "sub"), ("group", "ctx"), None),
        check_vma=False,
    )
```

```python
import functools
import math

import jax
import numpy as np
import jax.numpy as jnp
from jax import lax
from jax.experimental import pallas as pl
from jax.experimental.pallas import tpu as pltpu
from jax.sharding import PartitionSpec as P


ROW_TILE = 256
LOG2E = 1.4426950408889634
LN2 = 0.6931471805599453


def pair_kernel(scalar_ref, q_ref, k_ref, v_ref, upper_ref, *refs, mode, scale, rows, tile, offsets):
    for r in range(rows // tile):
        pair_rows(scalar_ref, q_ref, k_ref, v_ref, upper_ref, refs, mode, scale, r, tile, offsets)


def pair_rows(scalar_ref, q_all, k_ref, v_ref, upper_ref, refs, mode, scale, r, tile, offsets):
    diag = mode == "diag"
    rs = slice(r * tile, (r + 1) * tile)
    if mode in ("step", "final"):
        in_summed_ref, in_spent_ref, summed_ref, spent_ref = (ref.at[rs] for ref in refs)
    else:
        summed_ref = refs[0].at[rs]
    q_ref = q_all.at[rs]
    keys = upper_ref.shape[0]
    k_at, v_at = offsets
    score = (
        lax.dot_general(
            q_ref[...],
            k_ref[k_at : k_at + keys, :],
            (((1,), (1,)), ((), ())),
            preferred_element_type=jnp.float32,
        )
        * (scale * LOG2E)
        + scalar_ref[0] * LOG2E
    )
    spent = jnp.maximum(score, 0.0) + jnp.log2(1.0 + jnp.exp2(-jnp.abs(score)))
    if diag:
        row = r * tile + lax.broadcasted_iota(jnp.int32, (tile, keys), 0)
        col = lax.broadcasted_iota(jnp.int32, (tile, keys), 1)
        live = col < row
        spent = jnp.where(live, spent, 0.0)
    upper = upper_ref[...]
    high = spent.astype(jnp.bfloat16)
    low = (spent - high.astype(jnp.float32)).astype(jnp.bfloat16)
    later = jnp.dot(high, upper, preferred_element_type=jnp.float32) + jnp.dot(
        low, upper, preferred_element_type=jnp.float32
    )
    weight = jnp.exp2((score - spent) - later)
    if diag:
        weight = jnp.where(live, weight, 0.0)
    part = jnp.dot(
        weight.astype(jnp.bfloat16), v_ref[v_at : v_at + keys, :], preferred_element_type=jnp.float32
    )
    if mode == "far":
        summed_ref[...] = part.astype(summed_ref.dtype)
        return
    tot = (later[:, 0:1] + spent[:, 0:1]) * LN2
    if diag:
        summed_ref[...] = part
        refs[1].at[rs][...] = tot
        return
    use = scalar_ref[1] > 0.0
    before = in_spent_ref[...]
    summed_ref[...] = jnp.where(use, in_summed_ref[...] + jnp.exp(-before) * part, in_summed_ref[...])
    after = jnp.where(use, before + tot, before)
    if mode == "final":
        spent_ref[...] = jnp.broadcast_to(jnp.exp(-after), spent_ref.shape)
    else:
        spent_ref[...] = after


def payload_kernel(flag_ref, q_ref, k_ref, v_ref, sent_ref):
    rows = k_ref.shape[0]
    sent_ref[rows:, :] = v_ref[...]

    @pl.when(flag_ref[0] > 0.0)
    def _():
        sent_ref[:rows, :] = q_ref[...]

    @pl.when(flag_ref[0] <= 0.0)
    def _():
        sent_ref[:rows, :] = k_ref[...]


def payloads(flag, q, k, v):
    rows, width = k.shape
    block = pl.BlockSpec((rows, width), lambda i: (0, 0))
    both = pl.BlockSpec((2 * rows, width), lambda i: (0, 0))
    return pl.pallas_call(
        payload_kernel,
        grid=(1,),
        in_specs=[pl.BlockSpec(memory_space=pltpu.SMEM), block, block, block],
        out_specs=both,
        out_shape=jax.ShapeDtypeStruct((2 * rows, width), k.dtype),
    )(flag, q, k, v)


def finish_kernel(flag_ref, summed_ref, scale_ref, far_ref, out_ref):
    summed = summed_ref[...]

    @pl.when(flag_ref[0] > 0.0)
    def _():
        out_ref[...] = (summed + scale_ref[...] * far_ref[...].astype(jnp.float32)).astype(
            out_ref.dtype
        )

    @pl.when(flag_ref[0] <= 0.0)
    def _():
        out_ref[...] = summed.astype(out_ref.dtype)


def finished(flag, summed, scale, far):
    rows, width = summed.shape
    vmem = pl.BlockSpec(memory_space=pltpu.VMEM)
    return pl.pallas_call(
        finish_kernel,
        grid=(1,),
        in_specs=[pl.BlockSpec(memory_space=pltpu.SMEM), vmem, vmem, vmem],
        out_specs=pl.BlockSpec((rows, width), lambda i: (0, 0)),
        out_shape=jax.ShapeDtypeStruct((rows, width), jnp.bfloat16),
    )(flag, summed, scale, far)


def pair_terms(q, kv, upper, scalars, carried=None, mode="step", rows=None):
    width = q.shape[1]
    rows = q.shape[0] if rows is None else rows
    keys = upper.shape[0]
    tile = min(ROW_TILE, rows)
    if isinstance(kv, tuple):
        k, v = kv
        offsets = (0, 0)
    else:
        k = v = kv
        offsets = (0, keys)
    kernel = functools.partial(
        pair_kernel,
        mode=mode,
        scale=1.0 / math.sqrt(width),
        rows=rows,
        tile=tile,
        offsets=offsets,
    )
    flops = 2 * rows * keys * (2 * width + 2 * keys)
    vmem = pl.BlockSpec(memory_space=pltpu.VMEM)
    in_specs = [pl.BlockSpec(memory_space=pltpu.SMEM), vmem, vmem, vmem, vmem]
    args = [scalars, q, k, v, upper]
    if mode in ("step", "final"):
        in_specs += [vmem, vmem]
        args += list(carried)
    out_specs = [vmem]
    out_shape = [jax.ShapeDtypeStruct((rows, width), jnp.bfloat16 if mode == "far" else jnp.float32)]
    if mode == "final":
        out_specs.append(vmem)
        out_shape.append(jax.ShapeDtypeStruct((rows, width), jnp.float32))
    elif mode != "far":
        out_specs.append(vmem)
        out_shape.append(jax.ShapeDtypeStruct((rows, 1), jnp.float32))
    return pl.pallas_call(
        kernel,
        in_specs=in_specs,
        out_specs=out_specs,
        out_shape=out_shape,
        cost_estimate=pl.CostEstimate(
            flops=flops, transcendentals=3 * rows * keys, bytes_accessed=rows * width * 16
        ),
    )(*args)


def one_head(q_own, k_own, v_own, offset):
    count = lax.axis_size("ctx")
    place = lax.axis_index("ctx")
    up = [(i, (i + 1) % count) for i in range(count)]
    down = [(i, (i - 1) % count) for i in range(count)]
    rows = q_own.shape[0]
    keys = k_own.shape[0]
    upper = jnp.asarray(np.triu(np.ones((keys, keys), np.float32), 1).T, jnp.bfloat16)
    steps = jnp.arange(count, dtype=jnp.int32)
    table = jnp.stack(
        [jnp.broadcast_to(offset, (count,)), jnp.where(place >= steps, 1.0, 0.0)], axis=1
    ).astype(jnp.float32)
    last = place == count - 1
    flag = jnp.where(last, 1.0, 0.0).reshape(1).astype(jnp.float32)
    own_kv = (k_own, v_own)
    sent = payloads(flag, q_own, k_own, v_own)
    summed, spent = pair_terms(q_own, own_kv, upper, table[0], mode="diag")
    if count == 1:
        return summed.astype(jnp.bfloat16)
    if count == 2:
        kv = lax.ppermute(own_kv, "ctx", up)
        summed, spent = pair_terms(q_own, kv, upper, table[1], (summed, spent))
        return summed.astype(jnp.bfloat16)
    kv = lax.ppermute(sent, "ctx", up)
    far = pair_terms(kv, own_kv, upper, table[0], mode="far", rows=rows)[0]
    for step in range(1, count - 1):
        if step > 1:
            kv = lax.ppermute(kv, "ctx", up)
        if step < count - 2:
            summed, spent = pair_terms(q_own, kv, upper, table[step], (summed, spent))
    far = lax.ppermute(far, "ctx", down)
    summed, scale = pair_terms(q_own, kv, upper, table[count - 2], (summed, spent), mode="final")
    return finished(flag, summed, scale, far)


def on_device(queries, keys, values, stick_offset):
    results = []
    for h in range(queries.shape[0]):
        results.append(one_head(queries[h], keys[h], values[h], stick_offset[h]))
    return jnp.stack(results, axis=0)


def solution(mesh):
    placed = (
        P(("head", "sub"), ("group", "ctx"), None),
        P(("head", "sub"), ("group", "ctx"), None),
        P(("head", "sub"), ("group", "ctx"), None),
        P(("head", "sub")),
    )
    return jax.shard_map(
        on_device,
        mesh=mesh,
        in_specs=placed,
        out_specs=P(("head", "sub"), ("group", "ctx"), None),
        check_vma=False,
    )
```

```python
import functools
import math

import jax
import numpy as np
import jax.numpy as jnp
from jax import lax
from jax.experimental import pallas as pl
from jax.experimental.pallas import tpu as pltpu
from jax.sharding import PartitionSpec as P


ROW_TILE = 256
LOG2E = 1.4426950408889634
LN2 = 0.6931471805599453


def pair_kernel(scalar_ref, q_ref, kv_ref, upper_ref, *refs, mode, scale, rows, tile):
    for r in range(rows // tile):
        pair_rows(scalar_ref, q_ref, kv_ref, upper_ref, refs, mode, scale, r, tile)


def pair_rows(scalar_ref, q_all, kv_ref, upper_ref, refs, mode, scale, r, tile):
    diag = mode == "diag"
    rs = slice(r * tile, (r + 1) * tile)
    if mode in ("step", "final"):
        in_summed_ref, in_spent_ref, summed_ref, spent_ref = (ref.at[rs] for ref in refs)
    else:
        summed_ref = refs[0].at[rs]
    q_ref = q_all.at[rs]
    keys = kv_ref.shape[0] // 2
    score = (
        lax.dot_general(
            q_ref[...],
            kv_ref[:keys, :],
            (((1,), (1,)), ((), ())),
            preferred_element_type=jnp.float32,
        )
        * (scale * LOG2E)
        + scalar_ref[0] * LOG2E
    )
    spent = jnp.maximum(score, 0.0) + jnp.log2(1.0 + jnp.exp2(-jnp.abs(score)))
    if diag:
        row = r * tile + lax.broadcasted_iota(jnp.int32, (tile, keys), 0)
        col = lax.broadcasted_iota(jnp.int32, (tile, keys), 1)
        live = col < row
        spent = jnp.where(live, spent, 0.0)
    upper = upper_ref[...]
    high = spent.astype(jnp.bfloat16)
    low = (spent - high.astype(jnp.float32)).astype(jnp.bfloat16)
    later = jnp.dot(high, upper, preferred_element_type=jnp.float32) + jnp.dot(
        low, upper, preferred_element_type=jnp.float32
    )
    weight = jnp.exp2((score - spent) - later)
    if diag:
        weight = jnp.where(live, weight, 0.0)
    part = jnp.dot(weight.astype(jnp.bfloat16), kv_ref[keys:, :], preferred_element_type=jnp.float32)
    if mode == "far":
        summed_ref[...] = part.astype(summed_ref.dtype)
        return
    tot = (later[:, 0:1] + spent[:, 0:1]) * LN2
    if diag:
        summed_ref[...] = part
        refs[1].at[rs][...] = tot
        return
    use = scalar_ref[1] > 0.0
    before = in_spent_ref[...]
    summed_ref[...] = jnp.where(use, in_summed_ref[...] + jnp.exp(-before) * part, in_summed_ref[...])
    after = jnp.where(use, before + tot, before)
    if mode == "final":
        spent_ref[...] = jnp.broadcast_to(jnp.exp(-after), spent_ref.shape)
    else:
        spent_ref[...] = after


def payload_kernel(flag_ref, q_ref, k_ref, v_ref, own_ref, sent_ref):
    rows = k_ref.shape[0]
    own_ref[:rows, :] = k_ref[...]
    own_ref[rows:, :] = v_ref[...]
    sent_ref[rows:, :] = v_ref[...]

    @pl.when(flag_ref[0] > 0.0)
    def _():
        sent_ref[:rows, :] = q_ref[...]

    @pl.when(flag_ref[0] <= 0.0)
    def _():
        sent_ref[:rows, :] = k_ref[...]


def payloads(flag, q, k, v):
    rows, width = k.shape
    block = pl.BlockSpec((rows, width), lambda i: (0, 0))
    both = pl.BlockSpec((2 * rows, width), lambda i: (0, 0))
    shape = jax.ShapeDtypeStruct((2 * rows, width), k.dtype)
    return pl.pallas_call(
        payload_kernel,
        grid=(1,),
        in_specs=[pl.BlockSpec(memory_space=pltpu.SMEM), block, block, block],
        out_specs=[both, both],
        out_shape=[shape, shape],
    )(flag, q, k, v)


def fused_kernel(*refs, tasks, scale):
    scalar_ref, upper_ref = refs[0], refs[1]
    at = 2
    ins = []
    for mode, rows, tile in tasks:
        take = 2 + (2 if mode in ("step", "final") else 0)
        ins.append(refs[at : at + take])
        at += take
    for t, (mode, rows, tile) in enumerate(tasks):
        q_ref, kv_ref = ins[t][:2]
        carried = ins[t][2:]
        take = 1 if mode == "far" else 2
        outs = refs[at : at + take]
        at += take
        for r in range(rows // tile):
            pair_rows(
                scalar_ref.at[t], q_ref, kv_ref, upper_ref, tuple(carried) + tuple(outs),
                mode, scale, r, tile,
            )


def fused_terms(upper, tasks):
    vmem = pl.BlockSpec(memory_space=pltpu.VMEM)
    keys = upper.shape[0]
    scalars = jnp.stack([t["scalars"] for t in tasks])
    args = [scalars, upper]
    in_specs = [pl.BlockSpec(memory_space=pltpu.SMEM), vmem]
    out_specs, out_shape, statics = [], [], []
    flops = 0
    for t in tasks:
        q, kv, mode = t["q"], t["kv"], t["mode"]
        width = q.shape[1]
        rows = t.get("rows") or q.shape[0]
        args += [q, kv]
        in_specs += [vmem, vmem]
        if mode in ("step", "final"):
            args += list(t["carried"])
            in_specs += [vmem, vmem]
        out_specs.append(vmem)
        out_shape.append(jax.ShapeDtypeStruct((rows, width), jnp.bfloat16 if mode == "far" else jnp.float32))
        if mode != "far":
            out_specs.append(vmem)
            out_shape.append(
                jax.ShapeDtypeStruct((rows, width) if mode == "final" else (rows, 1), jnp.float32)
            )
        statics.append((mode, rows, min(ROW_TILE, rows)))
        flops += 2 * rows * keys * (2 * width + 2 * keys)
    kernel = functools.partial(fused_kernel, tasks=tuple(statics), scale=1.0 / math.sqrt(width))
    return pl.pallas_call(
        kernel,
        in_specs=in_specs,
        out_specs=out_specs,
        out_shape=out_shape,
        cost_estimate=pl.CostEstimate(
            flops=flops, transcendentals=3 * flops // (4 * width + 4 * keys), bytes_accessed=flops // 64
        ),
    )(*args)


def pair_terms(q, kv, upper, scalars, carried=None, mode="step", rows=None):
    width = q.shape[1]
    rows = q.shape[0] if rows is None else rows
    keys = kv.shape[0] // 2
    tile = min(ROW_TILE, rows)
    kernel = functools.partial(
        pair_kernel, mode=mode, scale=1.0 / math.sqrt(width), rows=rows, tile=tile
    )
    flops = 2 * rows * keys * (2 * width + 2 * keys)
    vmem = pl.BlockSpec(memory_space=pltpu.VMEM)
    in_specs = [pl.BlockSpec(memory_space=pltpu.SMEM), vmem, vmem, vmem]
    args = [scalars, q, kv, upper]
    if mode in ("step", "final"):
        in_specs += [vmem, vmem]
        args += list(carried)
    out_specs = [vmem]
    out_shape = [jax.ShapeDtypeStruct((rows, width), jnp.bfloat16 if mode == "far" else jnp.float32)]
    if mode == "final":
        out_specs.append(vmem)
        out_shape.append(jax.ShapeDtypeStruct((rows, width), jnp.float32))
    elif mode != "far":
        out_specs.append(vmem)
        out_shape.append(jax.ShapeDtypeStruct((rows, 1), jnp.float32))
    return pl.pallas_call(
        kernel,
        in_specs=in_specs,
        out_specs=out_specs,
        out_shape=out_shape,
        cost_estimate=pl.CostEstimate(
            flops=flops, transcendentals=3 * rows * keys, bytes_accessed=rows * width * 16
        ),
    )(*args)


def one_head(q_own, k_own, v_own, offset):
    count = lax.axis_size("ctx")
    place = lax.axis_index("ctx")
    up = [(i, (i + 1) % count) for i in range(count)]
    down = [(i, (i - 1) % count) for i in range(count)]
    rows = q_own.shape[0]
    keys = k_own.shape[0]
    upper = jnp.asarray(np.triu(np.ones((keys, keys), np.float32), 1).T, jnp.bfloat16)
    steps = jnp.arange(count, dtype=jnp.int32)
    table = jnp.stack(
        [jnp.broadcast_to(offset, (count,)), jnp.where(place >= steps, 1.0, 0.0)], axis=1
    ).astype(jnp.float32)
    last = place == count - 1
    own_kv, sent = payloads(jnp.where(last, 1.0, 0.0).reshape(1), q_own, k_own, v_own)
    summed, spent = pair_terms(q_own, own_kv, upper, table[0], mode="diag")
    if count == 1:
        return summed.astype(jnp.bfloat16)
    if count == 2:
        kv = lax.ppermute(own_kv, "ctx", up)
        summed, spent = pair_terms(q_own, kv, upper, table[1], (summed, spent))
        return summed.astype(jnp.bfloat16)
    kv = lax.ppermute(sent, "ctx", up)
    far_task = dict(q=kv, kv=own_kv, scalars=table[0], mode="far", rows=rows)
    if count > 3:
        far, summed, spent = fused_terms(
            upper,
            [far_task, dict(q=q_own, kv=kv, scalars=table[1], mode="step", carried=(summed, spent))],
        )
    else:
        (far,) = fused_terms(upper, [far_task])
    for step in range(2, count - 1):
        kv = lax.ppermute(kv, "ctx", up)
        if step < count - 2:
            summed, spent = pair_terms(q_own, kv, upper, table[step], (summed, spent))
    far = lax.ppermute(far, "ctx", down)
    summed, scale = pair_terms(
        q_own, kv, upper, table[count - 2], (summed, spent), mode="final"
    )
    out = jnp.where(last, summed + scale * far.astype(jnp.float32), summed)
    return out.astype(jnp.bfloat16)


def on_device(queries, keys, values, stick_offset):
    results = []
    for h in range(queries.shape[0]):
        results.append(one_head(queries[h], keys[h], values[h], stick_offset[h]))
    return jnp.stack(results, axis=0)


def solution(mesh):
    placed = (
        P(("head", "sub"), ("group", "ctx"), None),
        P(("head", "sub"), ("group", "ctx"), None),
        P(("head", "sub"), ("group", "ctx"), None),
        P(("head", "sub")),
    )
    return jax.shard_map(
        on_device,
        mesh=mesh,
        in_specs=placed,
        out_specs=P(("head", "sub"), ("group", "ctx"), None),
        check_vma=False,
    )
```

```python
import functools
import math

import jax
import numpy as np
import jax.numpy as jnp
from jax import lax
from jax.experimental import pallas as pl
from jax.experimental.pallas import tpu as pltpu
from jax.sharding import PartitionSpec as P


ROW_TILE = 256
LOG2E = 1.4426950408889634
LN2 = 0.6931471805599453


def pair_kernel(scalar_ref, q_ref, kv_ref, upper_ref, *refs, mode, scale, rows, tile):
    for r in range(rows // tile):
        pair_rows(scalar_ref, q_ref, kv_ref, upper_ref, refs, mode, scale, r, tile)


def pair_rows(scalar_ref, q_all, kv_ref, upper_ref, refs, mode, scale, r, tile):
    diag = mode == "diag"
    rs = slice(r * tile, (r + 1) * tile)
    if mode in ("step", "final"):
        in_summed_ref, in_spent_ref, summed_ref, spent_ref = (ref.at[rs] for ref in refs)
    else:
        summed_ref = refs[0].at[rs]
    q_ref = q_all.at[rs]
    keys = kv_ref.shape[0] // 2

    def terms():
        score = (
            lax.dot_general(
                q_ref[...],
                kv_ref[:keys, :],
                (((1,), (1,)), ((), ())),
                preferred_element_type=jnp.float32,
            )
            * (scale * LOG2E)
            + scalar_ref[0] * LOG2E
        )
        spent = jnp.maximum(score, 0.0) + jnp.log2(1.0 + jnp.exp2(-jnp.abs(score)))
        if diag:
            row = r * tile + lax.broadcasted_iota(jnp.int32, (tile, keys), 0)
            col = lax.broadcasted_iota(jnp.int32, (tile, keys), 1)
            live = col < row
            spent = jnp.where(live, spent, 0.0)
        upper = upper_ref[...]
        high = spent.astype(jnp.bfloat16)
        low = (spent - high.astype(jnp.float32)).astype(jnp.bfloat16)
        later = jnp.dot(high, upper, preferred_element_type=jnp.float32) + jnp.dot(
            low, upper, preferred_element_type=jnp.float32
        )
        weight = jnp.exp2((score - spent) - later)
        if diag:
            weight = jnp.where(live, weight, 0.0)
        part = jnp.dot(
            weight.astype(jnp.bfloat16), kv_ref[keys:, :], preferred_element_type=jnp.float32
        )
        return part, (later[:, 0:1] + spent[:, 0:1]) * LN2

    if diag:
        part, tot = terms()
        summed_ref[...] = part
        refs[1].at[rs][...] = tot
        return
    use = scalar_ref[1] > 0.0

    @pl.when(use)
    def _():
        part, tot = terms()
        if mode == "far":
            summed_ref[...] = part.astype(summed_ref.dtype)
            return
        before = in_spent_ref[...]
        summed_ref[...] = in_summed_ref[...] + jnp.exp(-before) * part
        after = before + tot
        if mode == "final":
            spent_ref[...] = jnp.broadcast_to(jnp.exp(-after), spent_ref.shape)
        else:
            spent_ref[...] = after

    @pl.when(jnp.logical_not(use))
    def _():
        if mode == "far":
            summed_ref[...] = jnp.zeros(summed_ref.shape, summed_ref.dtype)
            return
        summed_ref[...] = in_summed_ref[...]
        if mode == "final":
            spent_ref[...] = jnp.broadcast_to(jnp.exp(-in_spent_ref[...]), spent_ref.shape)
        else:
            spent_ref[...] = in_spent_ref[...]


def payload_kernel(flag_ref, q_ref, k_ref, v_ref, own_ref, sent_ref):
    rows = k_ref.shape[0]
    own_ref[:rows, :] = k_ref[...]
    own_ref[rows:, :] = v_ref[...]
    sent_ref[rows:, :] = v_ref[...]

    @pl.when(flag_ref[0] > 0.0)
    def _():
        sent_ref[:rows, :] = q_ref[...]

    @pl.when(flag_ref[0] <= 0.0)
    def _():
        sent_ref[:rows, :] = k_ref[...]


def payloads(flag, q, k, v):
    rows, width = k.shape
    block = pl.BlockSpec((rows, width), lambda i: (0, 0))
    both = pl.BlockSpec((2 * rows, width), lambda i: (0, 0))
    shape = jax.ShapeDtypeStruct((2 * rows, width), k.dtype)
    return pl.pallas_call(
        payload_kernel,
        grid=(1,),
        in_specs=[pl.BlockSpec(memory_space=pltpu.SMEM), block, block, block],
        out_specs=[both, both],
        out_shape=[shape, shape],
    )(flag, q, k, v)


def fused_kernel(*refs, tasks, scale):
    scalar_ref, upper_ref = refs[0], refs[1]
    at = 2
    ins = []
    for mode, rows, tile in tasks:
        take = 2 + (2 if mode in ("step", "final") else 0)
        ins.append(refs[at : at + take])
        at += take
    for t, (mode, rows, tile) in enumerate(tasks):
        q_ref, kv_ref = ins[t][:2]
        carried = ins[t][2:]
        take = 1 if mode == "far" else 2
        outs = refs[at : at + take]
        at += take
        for r in range(rows // tile):
            pair_rows(
                scalar_ref.at[t], q_ref, kv_ref, upper_ref, tuple(carried) + tuple(outs),
                mode, scale, r, tile,
            )


def fused_terms(upper, tasks):
    vmem = pl.BlockSpec(memory_space=pltpu.VMEM)
    keys = upper.shape[0]
    scalars = jnp.stack([t["scalars"] for t in tasks])
    args = [scalars, upper]
    in_specs = [pl.BlockSpec(memory_space=pltpu.SMEM), vmem]
    out_specs, out_shape, statics = [], [], []
    flops = 0
    for t in tasks:
        q, kv, mode = t["q"], t["kv"], t["mode"]
        width = q.shape[1]
        rows = t.get("rows") or q.shape[0]
        args += [q, kv]
        in_specs += [vmem, vmem]
        if mode in ("step", "final"):
            args += list(t["carried"])
            in_specs += [vmem, vmem]
        out_specs.append(vmem)
        out_shape.append(jax.ShapeDtypeStruct((rows, width), jnp.bfloat16 if mode == "far" else jnp.float32))
        if mode != "far":
            out_specs.append(vmem)
            out_shape.append(
                jax.ShapeDtypeStruct((rows, width) if mode == "final" else (rows, 1), jnp.float32)
            )
        statics.append((mode, rows, min(ROW_TILE, rows)))
        flops += 2 * rows * keys * (2 * width + 2 * keys)
    kernel = functools.partial(fused_kernel, tasks=tuple(statics), scale=1.0 / math.sqrt(width))
    return pl.pallas_call(
        kernel,
        in_specs=in_specs,
        out_specs=out_specs,
        out_shape=out_shape,
        cost_estimate=pl.CostEstimate(
            flops=flops, transcendentals=3 * flops // (4 * width + 4 * keys), bytes_accessed=flops // 64
        ),
    )(*args)


def pair_terms(q, kv, upper, scalars, carried=None, mode="step", rows=None):
    width = q.shape[1]
    rows = q.shape[0] if rows is None else rows
    keys = kv.shape[0] // 2
    tile = min(ROW_TILE, rows)
    kernel = functools.partial(
        pair_kernel, mode=mode, scale=1.0 / math.sqrt(width), rows=rows, tile=tile
    )
    flops = 2 * rows * keys * (2 * width + 2 * keys)
    vmem = pl.BlockSpec(memory_space=pltpu.VMEM)
    in_specs = [pl.BlockSpec(memory_space=pltpu.SMEM), vmem, vmem, vmem]
    args = [scalars, q, kv, upper]
    if mode in ("step", "final"):
        in_specs += [vmem, vmem]
        args += list(carried)
    out_specs = [vmem]
    out_shape = [jax.ShapeDtypeStruct((rows, width), jnp.bfloat16 if mode == "far" else jnp.float32)]
    if mode == "final":
        out_specs.append(vmem)
        out_shape.append(jax.ShapeDtypeStruct((rows, width), jnp.float32))
    elif mode != "far":
        out_specs.append(vmem)
        out_shape.append(jax.ShapeDtypeStruct((rows, 1), jnp.float32))
    return pl.pallas_call(
        kernel,
        in_specs=in_specs,
        out_specs=out_specs,
        out_shape=out_shape,
        cost_estimate=pl.CostEstimate(
            flops=flops, transcendentals=3 * rows * keys, bytes_accessed=rows * width * 16
        ),
    )(*args)


def one_head(q_own, k_own, v_own, offset):
    count = lax.axis_size("ctx")
    place = lax.axis_index("ctx")
    up = [(i, (i + 1) % count) for i in range(count)]
    down = [(i, (i - 1) % count) for i in range(count)]
    rows = q_own.shape[0]
    keys = k_own.shape[0]
    upper = jnp.asarray(np.triu(np.ones((keys, keys), np.float32), 1).T, jnp.bfloat16)
    steps = jnp.arange(count, dtype=jnp.int32)
    table = jnp.stack(
        [jnp.broadcast_to(offset, (count,)), jnp.where(place >= steps, 1.0, 0.0)], axis=1
    ).astype(jnp.float32)
    last = place == count - 1
    own_kv, sent = payloads(jnp.where(last, 1.0, 0.0).reshape(1), q_own, k_own, v_own)
    summed, spent = pair_terms(q_own, own_kv, upper, table[0], mode="diag")
    if count == 1:
        return summed.astype(jnp.bfloat16)
    if count == 2:
        kv = lax.ppermute(own_kv, "ctx", up)
        summed, spent = pair_terms(q_own, kv, upper, table[1], (summed, spent))
        return summed.astype(jnp.bfloat16)
    kv = lax.ppermute(sent, "ctx", up)
    far_gate = jnp.stack([offset, jnp.where(place == 0, 1.0, 0.0)]).astype(jnp.float32)
    far_task = dict(q=kv, kv=own_kv, scalars=far_gate, mode="far", rows=rows)
    if count > 3:
        far, summed, spent = fused_terms(
            upper,
            [far_task, dict(q=q_own, kv=kv, scalars=table[1], mode="step", carried=(summed, spent))],
        )
    else:
        (far,) = fused_terms(upper, [far_task])
    for step in range(2, count - 1):
        route = [(i, i + 1) for i in range(step - 1, count - 1)]
        route += [(i, i) for i in range(step - 1)] + [(count - 1, step - 1)]
        kv = lax.ppermute(kv, "ctx", route)
        if step < count - 2:
            summed, spent = pair_terms(q_own, kv, upper, table[step], (summed, spent))
    far = lax.ppermute(far, "ctx", down)
    summed, scale = pair_terms(q_own, kv, upper, table[count - 2], (summed, spent), mode="final")
    out = jnp.where(last, summed + scale * far.astype(jnp.float32), summed)
    return out.astype(jnp.bfloat16)


def on_device(queries, keys, values, stick_offset):
    results = []
    for h in range(queries.shape[0]):
        results.append(one_head(queries[h], keys[h], values[h], stick_offset[h]))
    return jnp.stack(results, axis=0)


def solution(mesh):
    placed = (
        P(("head", "sub"), ("group", "ctx"), None),
        P(("head", "sub"), ("group", "ctx"), None),
        P(("head", "sub"), ("group", "ctx"), None),
        P(("head", "sub")),
    )
    return jax.shard_map(
        on_device,
        mesh=mesh,
        in_specs=placed,
        out_specs=P(("head", "sub"), ("group", "ctx"), None),
        check_vma=False,
    )
```

```python
import functools
import math

import jax
import numpy as np
import jax.numpy as jnp
from jax import lax
from jax.experimental import pallas as pl
from jax.experimental.pallas import tpu as pltpu
from jax.sharding import PartitionSpec as P


ROW_TILE = 256
LOG2E = 1.4426950408889634
LN2 = 0.6931471805599453


def pair_kernel(scalar_ref, q_ref, kv_ref, upper_ref, *refs, mode, scale, rows, tile):
    for r in range(rows // tile):
        pair_rows(scalar_ref, q_ref, kv_ref, upper_ref, refs, mode, scale, r, tile)


def pair_rows(scalar_ref, q_all, kv_ref, upper_ref, refs, mode, scale, r, tile):
    diag = mode == "diag"
    rs = slice(r * tile, (r + 1) * tile)
    if mode in ("step", "final"):
        in_summed_ref, in_spent_ref, summed_ref, spent_ref = (ref.at[rs] for ref in refs)
    else:
        summed_ref = refs[0].at[rs]
    q_ref = q_all.at[rs]
    keys = kv_ref.shape[0] // 2

    def terms():
        score = (
            lax.dot_general(
                q_ref[...],
                kv_ref[:keys, :],
                (((1,), (1,)), ((), ())),
                preferred_element_type=jnp.float32,
            )
            * (scale * LOG2E)
            + scalar_ref[0] * LOG2E
        )
        spent = jnp.maximum(score, 0.0) + jnp.log2(1.0 + jnp.exp2(-jnp.abs(score)))
        if diag:
            row = r * tile + lax.broadcasted_iota(jnp.int32, (tile, keys), 0)
            col = lax.broadcasted_iota(jnp.int32, (tile, keys), 1)
            live = col < row
            spent = jnp.where(live, spent, 0.0)
        upper = upper_ref[...]
        high = spent.astype(jnp.bfloat16)
        low = (spent - high.astype(jnp.float32)).astype(jnp.bfloat16)
        later = jnp.dot(high, upper, preferred_element_type=jnp.float32) + jnp.dot(
            low, upper, preferred_element_type=jnp.float32
        )
        weight = jnp.exp2((score - spent) - later)
        if diag:
            weight = jnp.where(live, weight, 0.0)
        part = jnp.dot(
            weight.astype(jnp.bfloat16), kv_ref[keys:, :], preferred_element_type=jnp.float32
        )
        return part, (later[:, 0:1] + spent[:, 0:1]) * LN2

    if diag:
        part, tot = terms()
        summed_ref[...] = part
        refs[1].at[rs][...] = tot
        return
    use = scalar_ref[1] > 0.0

    @pl.when(use)
    def _():
        part, tot = terms()
        if mode == "far":
            summed_ref[...] = part.astype(summed_ref.dtype)
            return
        before = in_spent_ref[...]
        summed_ref[...] = in_summed_ref[...] + jnp.exp(-before) * part
        after = before + tot
        if mode == "final":
            spent_ref[...] = jnp.broadcast_to(jnp.exp(-after), spent_ref.shape)
        else:
            spent_ref[...] = after

    @pl.when(jnp.logical_not(use))
    def _():
        if mode == "far":
            summed_ref[...] = jnp.zeros(summed_ref.shape, summed_ref.dtype)
            return
        summed_ref[...] = in_summed_ref[...]
        if mode == "final":
            spent_ref[...] = jnp.broadcast_to(jnp.exp(-in_spent_ref[...]), spent_ref.shape)
        else:
            spent_ref[...] = in_spent_ref[...]


def payload_kernel(flag_ref, q_ref, k_ref, v_ref, own_ref, sent_ref):
    rows = k_ref.shape[0]
    own_ref[:rows, :] = k_ref[...]
    own_ref[rows:, :] = v_ref[...]
    sent_ref[rows:, :] = v_ref[...]

    @pl.when(flag_ref[0] > 0.0)
    def _():
        sent_ref[:rows, :] = q_ref[...]

    @pl.when(flag_ref[0] <= 0.0)
    def _():
        sent_ref[:rows, :] = k_ref[...]


def payloads(flag, q, k, v):
    rows, width = k.shape
    block = pl.BlockSpec((rows, width), lambda i: (0, 0))
    both = pl.BlockSpec((2 * rows, width), lambda i: (0, 0))
    shape = jax.ShapeDtypeStruct((2 * rows, width), k.dtype)
    return pl.pallas_call(
        payload_kernel,
        grid=(1,),
        in_specs=[pl.BlockSpec(memory_space=pltpu.SMEM), block, block, block],
        out_specs=[both, both],
        out_shape=[shape, shape],
    )(flag, q, k, v)


def fused_kernel(*refs, tasks, scale):
    scalar_ref, upper_ref = refs[0], refs[1]
    at = 2
    ins = []
    for mode, rows, tile in tasks:
        take = 2 + (2 if mode in ("step", "final") else 0)
        ins.append(refs[at : at + take])
        at += take
    for t, (mode, rows, tile) in enumerate(tasks):
        q_ref, kv_ref = ins[t][:2]
        carried = ins[t][2:]
        take = 1 if mode == "far" else 2
        outs = refs[at : at + take]
        at += take
        for r in range(rows // tile):
            pair_rows(
                scalar_ref.at[t], q_ref, kv_ref, upper_ref, tuple(carried) + tuple(outs),
                mode, scale, r, tile,
            )


def fused_terms(upper, tasks):
    vmem = pl.BlockSpec(memory_space=pltpu.VMEM)
    keys = upper.shape[0]
    scalars = jnp.stack([t["scalars"] for t in tasks])
    args = [scalars, upper]
    in_specs = [pl.BlockSpec(memory_space=pltpu.SMEM), vmem]
    out_specs, out_shape, statics = [], [], []
    flops = 0
    for t in tasks:
        q, kv, mode = t["q"], t["kv"], t["mode"]
        width = q.shape[1]
        rows = t.get("rows") or q.shape[0]
        args += [q, kv]
        in_specs += [vmem, vmem]
        if mode in ("step", "final"):
            args += list(t["carried"])
            in_specs += [vmem, vmem]
        out_specs.append(vmem)
        out_shape.append(jax.ShapeDtypeStruct((rows, width), jnp.bfloat16 if mode == "far" else jnp.float32))
        if mode != "far":
            out_specs.append(vmem)
            out_shape.append(
                jax.ShapeDtypeStruct((rows, width) if mode == "final" else (rows, 1), jnp.float32)
            )
        statics.append((mode, rows, min(ROW_TILE, rows)))
        flops += 2 * rows * keys * (2 * width + 2 * keys)
    kernel = functools.partial(fused_kernel, tasks=tuple(statics), scale=1.0 / math.sqrt(width))
    return pl.pallas_call(
        kernel,
        in_specs=in_specs,
        out_specs=out_specs,
        out_shape=out_shape,
        cost_estimate=pl.CostEstimate(
            flops=flops, transcendentals=3 * flops // (4 * width + 4 * keys), bytes_accessed=flops // 64
        ),
    )(*args)


def pair_terms(q, kv, upper, scalars, carried=None, mode="step", rows=None):
    width = q.shape[1]
    rows = q.shape[0] if rows is None else rows
    keys = kv.shape[0] // 2
    tile = min(ROW_TILE, rows)
    kernel = functools.partial(
        pair_kernel, mode=mode, scale=1.0 / math.sqrt(width), rows=rows, tile=tile
    )
    flops = 2 * rows * keys * (2 * width + 2 * keys)
    vmem = pl.BlockSpec(memory_space=pltpu.VMEM)
    in_specs = [pl.BlockSpec(memory_space=pltpu.SMEM), vmem, vmem, vmem]
    args = [scalars, q, kv, upper]
    if mode in ("step", "final"):
        in_specs += [vmem, vmem]
        args += list(carried)
    out_specs = [vmem]
    out_shape = [jax.ShapeDtypeStruct((rows, width), jnp.bfloat16 if mode == "far" else jnp.float32)]
    if mode == "final":
        out_specs.append(vmem)
        out_shape.append(jax.ShapeDtypeStruct((rows, width), jnp.float32))
    elif mode != "far":
        out_specs.append(vmem)
        out_shape.append(jax.ShapeDtypeStruct((rows, 1), jnp.float32))
    return pl.pallas_call(
        kernel,
        in_specs=in_specs,
        out_specs=out_specs,
        out_shape=out_shape,
        cost_estimate=pl.CostEstimate(
            flops=flops, transcendentals=3 * rows * keys, bytes_accessed=rows * width * 16
        ),
    )(*args)


def one_head(q_own, k_own, v_own, offset):
    count = lax.axis_size("ctx")
    place = lax.axis_index("ctx")
    up = [(i, (i + 1) % count) for i in range(count)]
    rows = q_own.shape[0]
    keys = k_own.shape[0]
    upper = jnp.asarray(np.triu(np.ones((keys, keys), np.float32), 1).T, jnp.bfloat16)
    steps = jnp.arange(count, dtype=jnp.int32)
    table = jnp.stack(
        [jnp.broadcast_to(offset, (count,)), jnp.where(place >= steps, 1.0, 0.0)], axis=1
    ).astype(jnp.float32)
    last = place == count - 1
    own_kv, sent = payloads(jnp.where(last, 1.0, 0.0).reshape(1), q_own, k_own, v_own)
    summed, spent = pair_terms(q_own, own_kv, upper, table[0], mode="diag")
    if count == 1:
        return summed.astype(jnp.bfloat16)
    if count == 2:
        kv = lax.ppermute(own_kv, "ctx", up)
        summed, spent = pair_terms(q_own, kv, upper, table[1], (summed, spent))
        return summed.astype(jnp.bfloat16)
    kv = lax.ppermute(sent, "ctx", up)
    far_gate = jnp.stack([offset, jnp.where(place == 0, 1.0, 0.0)]).astype(jnp.float32)
    far_task = dict(q=kv, kv=own_kv, scalars=far_gate, mode="far", rows=rows)
    if count > 3:
        far, summed, spent = fused_terms(
            upper,
            [far_task, dict(q=q_own, kv=kv, scalars=table[1], mode="step", carried=(summed, spent))],
        )
    else:
        (far,) = fused_terms(upper, [far_task])
    for step in range(2, count - 1):
        route = [(i, i + 1) for i in range(step - 1, count - 1)]
        route += [(i, i) for i in range(step - 1)] + [(count - 1, step - 1)]
        kv = lax.ppermute(kv, "ctx", route)
        if step < count - 2:
            summed, spent = pair_terms(q_own, kv, upper, table[step], (summed, spent))
    swap = [(0, count - 1), (count - 1, 0)]
    middle = list(range(1, count - 1))
    swap += [(a, b) for a, b in zip(middle[0::2], middle[1::2])]
    swap += [(b, a) for a, b in zip(middle[0::2], middle[1::2])]
    if len(middle) % 2:
        swap.append((middle[-1], middle[-1]))
    far = lax.ppermute(far, "ctx", swap)
    summed, scale = pair_terms(q_own, kv, upper, table[count - 2], (summed, spent), mode="final")
    out = jnp.where(last, summed + scale * far.astype(jnp.float32), summed)
    return out.astype(jnp.bfloat16)


def on_device(queries, keys, values, stick_offset):
    results = []
    for h in range(queries.shape[0]):
        results.append(one_head(queries[h], keys[h], values[h], stick_offset[h]))
    return jnp.stack(results, axis=0)


def solution(mesh):
    placed = (
        P(("head", "sub"), ("group", "ctx"), None),
        P(("head", "sub"), ("group", "ctx"), None),
        P(("head", "sub"), ("group", "ctx"), None),
        P(("head", "sub")),
    )
    return jax.shard_map(
        on_device,
        mesh=mesh,
        in_specs=placed,
        out_specs=P(("head", "sub"), ("group", "ctx"), None),
        check_vma=False,
    )
```
